256 devices in a mesh: section: 2 (over core), patch: 4 (over y), req: 32 (over z, x).
Axes of the slice: x: 4, y: 4, z: 8, core: 2. Of those that a mesh axis runs over, the one named last changes fastest.
Arguments:
- hidden: bfloat16 [64, 1024, 1536], P('req', 'patch'), may hold values from -6 to 6
- w_qkv: bfloat16 [2, 1536, 2304], P('section', ('patch', 'req')), may hold values from -0.15625 to 0.15625
- w_out: bfloat16 [2, 768, 1536], P('section', ('patch', 'req')), may hold values from -0.21875 to 0.21875
- modulation: float32 [2, 64, 3, 1536], P('section', 'req'), may hold values from -3 to 3
- text_kv: bfloat16 [2, 64, 160, 1536], P('section', 'req'), may hold values from -1000 to 1000
- text_lengths: int32 [64], P('req'), may hold values from 77 to 154, as said below
- stale_kv: bfloat16 [2, 64, 1024, 1536], P('section', 'req', 'patch'), may hold values from -48 to 48
- held_hidden: bfloat16 [2, 64, 96, 1536], P('section', 'req', 'patch'), may hold values from -6 to 6
- recompute_rows: int32 [2, 64, 96], P('section', 'req', 'patch'), may hold values from 0 to 255, as said below
- coefficients: float32 [64, 2], P('req'), may hold values from 0.5 to 1.5
Outputs:
- latents: float32 [64, 1024, 1536], P('req', 'patch', 'section')
- cache: bfloat16 [2, 64, 1024, 1536], P('section', 'req', 'patch')
The draws below stay inside these ranges and needn't reach their ends.
Inputs may be any that keep to these rules, and one draw needn't show every extreme that they name: `text_lengths`: some request has exactly 154 text tokens and some exactly 77. `recompute_rows`: the row numbers listed for one layer, request and patch are distinct.
All inputs are finite; a program needn't handle non-finite values.
Results may differ from the reference program's by a relative error of at most 0.025.
Values may be sent and summed in bfloat16 or wider, within the bound.
No kernel may reach another device: no remote copies, remote signals or barrier semaphores. Data moves between devices by JAX's collectives and lax.ppermute only.
A program may use at most 128 MiB of HBM per device.

```python
import jax
import jax.numpy as jnp
from jax import lax

D = 1536
HEAD = 64
HEADS = 12
PATCH_ROWS = 256
RECOMP = 24
TXT_MIN = 77
TXT_MAX = 154
PATCHES = 4
IMG = 1024
HK = 768
TXT = 160
REQUESTS = 64


def draw_text_kv(key, part):
    base = jax.random.normal(jax.random.fold_in(key, 11), (2, REQUESTS, TXT, 2 * HEADS * HEAD), jnp.float32)
    return jnp.clip(base, -1000.0, 1000.0).astype(jnp.bfloat16)


def draw_text_lengths(key, part):
    drawn = jax.random.randint(jax.random.fold_in(key, 21), (REQUESTS,), TXT_MIN, TXT_MAX + 1)
    drawn = drawn.at[0].set(TXT_MAX)
    return drawn.at[REQUESTS - 1].set(TXT_MIN).astype(jnp.int32)


def draw_recompute_rows(key, part):
    group_keys = jax.random.split(jax.random.fold_in(key, 31), 2 * REQUESTS * PATCHES)
    picked = jax.vmap(lambda group_key: jax.random.permutation(group_key, PATCH_ROWS)[:RECOMP])(group_keys)
    return picked.reshape(2, REQUESTS, PATCHES * RECOMP).astype(jnp.int32)


def draw_stale_kv(key, part):
    shape_keys = (2, REQUESTS, IMG, HEADS * HEAD)
    key_part = jax.random.normal(jax.random.fold_in(key, 41), shape_keys, jnp.float32)
    value_part = 8.0 * jax.random.normal(jax.random.fold_in(key, 42), shape_keys, jnp.float32)
    key_part = jnp.clip(key_part, -6.0, 6.0)
    value_part = jnp.clip(value_part, -48.0, 48.0)
    return jnp.concatenate([key_part, value_part], axis=-1).astype(jnp.bfloat16)


def steps_of(own_key, extent, cuts, low, largest):
    loudness = 1.0
    for dim, blocks in cuts:
        steps = jax.random.uniform(jax.random.fold_in(jax.random.fold_in(own_key, 6), dim), (blocks,), jnp.float32, low / len(cuts), largest / len(cuts))
        loudness = loudness * jnp.repeat(jnp.exp(steps), extent[dim] // blocks).reshape((-1,) + (1,) * (len(extent) - 1 - dim))
    return loudness


def scatter_about(rng, extent, width, bound, cuts=(), held_as=jnp.bfloat16):
    gain = steps_of(rng, extent, cuts, -0.22, 0.18) if cuts else 1.0
    result = jax.random.normal(rng, extent, jnp.float32) * width * gain
    return jnp.minimum(jnp.maximum(result, -bound), bound).astype(held_as)


def setup_inputs(seed: int = 0) -> dict:
    keys = jax.random.split(jax.random.key(seed), 11)
    return {
        "hidden": scatter_about(keys[0], (REQUESTS, IMG, D), 1.0, 6.0, ((0, 32), (1, 4))),
        "w_qkv": scatter_about(keys[1], (2, D, 3 * HK), D ** -0.5, 0.15625, ((0, 2), (1, 128))),
        "w_out": scatter_about(keys[2], (2, HK, D), HK ** -0.5, 0.21875, ((0, 2), (1, 128))),
        "modulation": scatter_about(keys[3], (2, REQUESTS, 3, D), 0.5, 3.0, ((0, 2), (1, 32)), jnp.float32),
        "text_kv": draw_text_kv(jax.random.fold_in(keys[10], 71), 0),
        "text_lengths": draw_text_lengths(jax.random.fold_in(keys[10], 71), 0),
        "stale_kv": draw_stale_kv(jax.random.fold_in(keys[10], 71), 0),
        "held_hidden": scatter_about(keys[7], (2, REQUESTS, PATCHES * RECOMP, D), 1.0, 6.0, ((0, 2), (1, 32), (2, 4))),
        "recompute_rows": draw_recompute_rows(jax.random.fold_in(keys[10], 71), 0),
        "coefficients": jnp.clip(0.5 + 1.0 * jax.random.uniform(keys[9], (REQUESTS, 2), jnp.float32) ** steps_of(keys[9], (REQUESTS, 2), ((0, 32),), -0.2, 0.2), 0.5, 1.5),
    }


norm_eps = 1e-06
score_scale = 0.125

def modulate(row_block, shift_row, scale_row):
    values = row_block.astype(jnp.float32)
    centre = values - lax.optimization_barrier(jnp.mean(values, axis=-1, keepdims=True))
    spread = lax.optimization_barrier(jnp.mean(centre * centre, axis=-1, keepdims=True))
    return (centre * lax.rsqrt(spread + norm_eps) * (1.0 + scale_row) + shift_row).astype(jnp.bfloat16)

def attend(queries, key_rows, value_rows, usable):
    row_count = queries.shape[0]
    feature_count = queries.shape[1]
    query_heads = queries.astype(jnp.float32).reshape(row_count, HEADS, feature_count // HEADS)
    key_heads = key_rows.astype(jnp.float32).reshape(key_rows.shape[0], HEADS, feature_count // HEADS)
    value_heads = value_rows.astype(jnp.float32).reshape(value_rows.shape[0], HEADS, feature_count // HEADS)
    scores = jnp.einsum('qhd,khd->hqk', query_heads, key_heads) * score_scale
    scores = jnp.where(usable[None, None, :], scores, -1e+30)
    row_max = lax.optimization_barrier(jnp.max(scores, axis=-1, keepdims=True))
    exp_scores = jnp.exp(scores - row_max)
    soft_weights = (exp_scores / lax.optimization_barrier(jnp.sum(exp_scores, axis=-1, keepdims=True))).astype(jnp.bfloat16)
    attended = jnp.einsum('hqk,khd->qhd', soft_weights.astype(jnp.float32), value_heads)
    return attended.reshape(row_count, feature_count).astype(jnp.bfloat16)

def run_layer(layer_input, mod_rows, qkv_weight, out_weight, text_rows, text_count, stale_block, held_rows, redo_index):
    head_width = out_weight.shape[0]
    held_norm = modulate(held_rows, mod_rows[0], mod_rows[1])
    redone = jnp.dot(held_norm, qkv_weight[:, head_width:], preferred_element_type=jnp.float32).astype(jnp.bfloat16)
    pieces = []
    for patch_number in range(PATCHES):
        stale_piece = stale_block[patch_number * PATCH_ROWS:(patch_number + 1) * PATCH_ROWS]
        first_row = patch_number * RECOMP
        pieces.append(stale_piece.at[redo_index[first_row:first_row + RECOMP]].set(redone[first_row:first_row + RECOMP]))
    normed = modulate(layer_input, mod_rows[0], mod_rows[1])
    projected = jnp.dot(normed, qkv_weight, preferred_element_type=jnp.float32).astype(jnp.bfloat16)
    fresh_all = projected[:, head_width:]
    usable = jnp.concatenate([jnp.arange(TXT) < text_count, jnp.ones((IMG,), jnp.bool_)])
    outputs = []
    for patch_number in range(PATCHES):
        row_start = patch_number * PATCH_ROWS
        image_rows = jnp.concatenate(pieces[:patch_number] + [fresh_all[row_start:row_start + PATCH_ROWS]] + pieces[patch_number + 1:], axis=0)
        context = jnp.concatenate([text_rows, image_rows], axis=0)
        attended = attend(projected[row_start:row_start + PATCH_ROWS, :head_width], context[:, :head_width], context[:, head_width:], usable)
        update = jnp.dot(attended, out_weight, preferred_element_type=jnp.float32)
        outputs.append((layer_input[row_start:row_start + PATCH_ROWS].astype(jnp.float32) + mod_rows[2] * update).astype(jnp.bfloat16))
    return (jnp.concatenate(outputs, axis=0), fresh_all)

def reference(hidden, w_qkv, w_out, modulation, text_kv, text_lengths, stale_kv, held_hidden, recompute_rows, coefficients):
    per_request = (hidden, jnp.moveaxis(modulation, 1, 0), jnp.moveaxis(text_kv, 1, 0), text_lengths, jnp.moveaxis(stale_kv, 1, 0), jnp.moveaxis(held_hidden, 1, 0), jnp.moveaxis(recompute_rows, 1, 0), coefficients)

    def one_request(bundle):
        source, mod_sets, text_sets, text_count, stales, held_sets, redo_sets, coef_pair = bundle
        layer_input = source
        caches = []
        for layer_index in range(2):
            layer_input, fresh_all = run_layer(layer_input, mod_sets[layer_index], w_qkv[layer_index], w_out[layer_index], text_sets[layer_index], text_count, stales[layer_index], held_sets[layer_index], redo_sets[layer_index])
            caches.append(fresh_all)
        latents = coef_pair[0] * source.astype(jnp.float32) + coef_pair[1] * layer_input.astype(jnp.float32)
        return (latents, jnp.stack(caches))
    latents, cache = lax.map(one_request, per_request)
    return (latents, jnp.moveaxis(cache, 1, 0))
```

```python
import jax
import jax.numpy as jnp
from jax import lax
from jax.sharding import PartitionSpec as P

HEADS = 12


norm_eps = 1e-06
score_scale = 0.125


def shifted(block, axis, distance):
    devices = range(lax.axis_size(axis))
    route = [(i - distance, i) for i in devices if i - distance in devices]
    return lax.ppermute(block, axis, route)


def rotated(block, axis, distance):
    size = lax.axis_size(axis)
    return lax.ppermute(block, axis, [(i, (i + distance) % size) for i in range(size)])


def modulate(row_block, shift_row, scale_row):
    values = row_block.astype(jnp.float32)
    centre = values - jnp.mean(values, axis=-1, keepdims=True)
    spread = jnp.mean(centre * centre, axis=-1, keepdims=True)
    return (centre * lax.rsqrt(spread + norm_eps) * (1.0 + scale_row) + shift_row).astype(
        jnp.bfloat16
    )


def attend(queries, key_rows, value_rows, usable):
    row_count = queries.shape[0]
    feature_count = queries.shape[1]
    query_heads = queries.reshape(row_count, HEADS, feature_count // HEADS)
    key_heads = key_rows.reshape(key_rows.shape[0], HEADS, feature_count // HEADS)
    value_heads = value_rows.reshape(value_rows.shape[0], HEADS, feature_count // HEADS)
    scores = (
        jnp.einsum("qhd,khd->hqk", query_heads, key_heads, preferred_element_type=jnp.float32)
        * score_scale
    )
    scores = jnp.where(usable[None, None, :], scores, -1e30)
    row_max = jnp.max(scores, axis=-1, keepdims=True)
    exp_scores = jnp.exp(scores - row_max)
    soft_weights = (exp_scores / jnp.sum(exp_scores, axis=-1, keepdims=True)).astype(jnp.bfloat16)
    attended = jnp.einsum(
        "hqk,khd->qhd", soft_weights, value_heads, preferred_element_type=jnp.float32
    )
    return attended.reshape(row_count, feature_count).astype(jnp.bfloat16)


def gather_weights(w_qkv, w_out):
    qkv_shard = w_qkv[0]
    out_shard = w_out[0]
    qkv_rows, qkv_cols = qkv_shard.shape
    out_rows, out_cols = out_shard.shape
    flat = jnp.concatenate([qkv_shard.reshape(-1), out_shard.reshape(-1)]).reshape(-1, 128)
    gathered = lax.all_gather(flat, "patch", axis=0, tiled=True)
    gathered = lax.all_gather(gathered, "req", axis=0, tiled=True)
    patches = lax.axis_size("patch")
    requests = lax.axis_size("req")
    gathered = gathered.reshape(requests, patches, -1).transpose(1, 0, 2)
    gathered = gathered.reshape(patches * requests, -1)
    qkv_size = qkv_rows * qkv_cols
    full_qkv = gathered[:, :qkv_size].reshape(-1, qkv_cols)
    full_out = gathered[:, qkv_size:].reshape(-1, out_cols)
    return full_qkv, full_out


def body(
    hidden,
    w_qkv,
    w_out,
    modulation,
    text_kv,
    text_lengths,
    stale_kv,
    held_hidden,
    recompute_rows,
    coefficients,
):
    section_index = lax.axis_index("section")
    patch_count = lax.axis_size("patch")
    request_count = hidden.shape[0]
    patch_rows = hidden.shape[1]
    model_width = hidden.shape[2]
    held_count = held_hidden.shape[2]
    text_slots = text_kv.shape[2]

    index_row = jnp.zeros((request_count, 1, model_width), jnp.bfloat16)
    index_row = index_row.at[:, 0, :held_count].set(recompute_rows[0].astype(jnp.bfloat16))
    payload = jnp.concatenate([stale_kv[0], held_hidden[0], index_row], axis=1)
    arrivals = [rotated(payload, "patch", distance) for distance in range(1, patch_count)]

    full_qkv, full_out = gather_weights(w_qkv, w_out)
    head_width = full_out.shape[0]
    key_weights = full_qkv[:, head_width:]

    others = []
    for slot in range(request_count):
        mod_rows = modulation[0, slot]
        pieces = []
        for arrival in arrivals:
            stale_rows = arrival[slot, :patch_rows]
            held_rows = arrival[slot, patch_rows : patch_rows + held_count]
            redo_index = arrival[slot, patch_rows + held_count, :held_count].astype(jnp.int32)
            held_norm = modulate(held_rows, mod_rows[0], mod_rows[1])
            redone = jnp.dot(held_norm, key_weights, preferred_element_type=jnp.float32).astype(
                jnp.bfloat16
            )
            pieces.append(stale_rows.at[redo_index].set(redone))
        others.append(jnp.concatenate(pieces, axis=0))
    others = jnp.stack(others)

    def process(layer_input, slot_index):
        mod_rows = lax.dynamic_index_in_dim(modulation[0], slot_index, 0, keepdims=False)
        text_rows = lax.dynamic_index_in_dim(text_kv[0], slot_index, 0, keepdims=False)
        text_count = lax.dynamic_index_in_dim(text_lengths, slot_index, 0, keepdims=False)
        other_rows = lax.dynamic_index_in_dim(others, slot_index, 0, keepdims=False)
        normed = modulate(layer_input, mod_rows[0], mod_rows[1])
        projected = jnp.dot(normed, full_qkv, preferred_element_type=jnp.float32).astype(
            jnp.bfloat16
        )
        fresh_rows = projected[:, head_width:]
        context = jnp.concatenate([text_rows, fresh_rows, other_rows], axis=0)
        usable = jnp.concatenate(
            [
                jnp.arange(text_slots) < text_count,
                jnp.ones((context.shape[0] - text_slots,), jnp.bool_),
            ]
        )
        attended = attend(
            projected[:, :head_width], context[:, :head_width], context[:, head_width:], usable
        )
        update = jnp.dot(attended, full_out, preferred_element_type=jnp.float32)
        layer_out = (layer_input.astype(jnp.float32) + mod_rows[2] * update).astype(jnp.bfloat16)
        return layer_out, fresh_rows

    first_section = section_index == 0
    half_width = model_width // 2

    out_1, fresh_1 = process(hidden[0], 0)
    received_1 = shifted(out_1, "section", 1)
    input_2 = jnp.where(first_section, hidden[1], received_1)
    out_2, fresh_2 = process(input_2, jnp.where(first_section, 1, 0))
    returned_a = shifted(out_2[:, :half_width], "section", -1)
    received_2 = shifted(out_2, "section", 1)
    out_3, fresh_3 = process(received_2, 1)
    returned_b = shifted(out_3[:, :half_width], "section", -1)

    cache = jnp.stack(
        [jnp.where(first_section, fresh_1, fresh_2), jnp.where(first_section, fresh_2, fresh_3)]
    )
    last_out = jnp.stack([out_2, out_3])
    returned = jnp.stack([returned_a, returned_b])
    own_half = jnp.where(first_section, returned, last_out[:, :, half_width:])
    source_half = lax.dynamic_slice_in_dim(hidden, section_index * half_width, half_width, 2)
    latents = coefficients[:, 0][:, None, None] * source_half.astype(jnp.float32) + coefficients[
        :, 1
    ][:, None, None] * own_half.astype(jnp.float32)
    return (latents, cache[None])


def solution(mesh):
    return jax.shard_map(
        body,
        mesh=mesh,
        in_specs=(
            P("req", "patch", None),
            P("section", ("patch", "req"), None),
            P("section", ("patch", "req"), None),
            P("section", "req", None, None),
            P("section", "req", None, None),
            P("req"),
            P("section", "req", "patch", None),
            P("section", "req", "patch", None),
            P("section", "req", "patch"),
            P("req", None),
        ),
        out_specs=(P("req", "patch", "section"), P("section", "req", "patch", None)),
        check_vma=False,
    )
```

```python
import jax
import jax.numpy as jnp
from jax import lax
from jax.sharding import PartitionSpec as P

HEADS = 12


norm_eps = 1e-06
score_scale = 0.125


def shifted(block, axis, distance):
    devices = range(lax.axis_size(axis))
    route = [(i - distance, i) for i in devices if i - distance in devices]
    return lax.ppermute(block, axis, route)


def rotated(block, axis, distance):
    size = lax.axis_size(axis)
    return lax.ppermute(block, axis, [(i, (i + distance) % size) for i in range(size)])


def modulate(row_block, shift_row, scale_row):
    values = row_block.astype(jnp.float32)
    centre = values - jnp.mean(values, axis=-1, keepdims=True)
    spread = jnp.mean(centre * centre, axis=-1, keepdims=True)
    return (centre * lax.rsqrt(spread + norm_eps) * (1.0 + scale_row) + shift_row).astype(
        jnp.bfloat16
    )


def attend(queries, key_rows, value_rows, usable):
    row_count = queries.shape[0]
    feature_count = queries.shape[1]
    query_heads = queries.reshape(row_count, HEADS, feature_count // HEADS)
    key_heads = key_rows.reshape(key_rows.shape[0], HEADS, feature_count // HEADS)
    value_heads = value_rows.reshape(value_rows.shape[0], HEADS, feature_count // HEADS)
    scores = (
        jnp.einsum("qhd,khd->hqk", query_heads, key_heads, preferred_element_type=jnp.float32)
        * score_scale
    )
    scores = jnp.where(usable[None, None, :], scores, -1e30)
    row_max = jnp.max(scores, axis=-1, keepdims=True)
    exp_scores = jnp.exp(scores - row_max)
    soft_weights = (exp_scores / jnp.sum(exp_scores, axis=-1, keepdims=True)).astype(jnp.bfloat16)
    attended = jnp.einsum(
        "hqk,khd->qhd", soft_weights, value_heads, preferred_element_type=jnp.float32
    )
    return attended.reshape(row_count, feature_count).astype(jnp.bfloat16)


def gather_weights(w_qkv, w_out):
    qkv_shard = w_qkv[0]
    out_shard = w_out[0]
    qkv_rows, qkv_cols = qkv_shard.shape
    out_rows, out_cols = out_shard.shape
    out_folded = out_shard.reshape(-1, qkv_cols)
    chunk = jnp.concatenate([qkv_shard, out_folded], axis=0)
    chunk_rows = chunk.shape[0]
    gathered = lax.all_gather(chunk, "patch", axis=0, tiled=True)
    gathered = lax.all_gather(gathered, "req", axis=0, tiled=True)
    patches = lax.axis_size("patch")
    requests = lax.axis_size("req")
    gathered = gathered.reshape(requests, patches, chunk_rows, qkv_cols)
    full_qkv = gathered[:, :, :qkv_rows].transpose(1, 0, 2, 3).reshape(-1, qkv_cols)
    full_out = (
        gathered[:, :, qkv_rows:].transpose(1, 0, 2, 3).reshape(patches * requests, -1)
    ).reshape(-1, out_cols)
    return full_qkv, full_out


def body(
    hidden,
    w_qkv,
    w_out,
    modulation,
    text_kv,
    text_lengths,
    stale_kv,
    held_hidden,
    recompute_rows,
    coefficients,
):
    section_index = lax.axis_index("section")
    patch_count = lax.axis_size("patch")
    request_count = hidden.shape[0]
    patch_rows = hidden.shape[1]
    model_width = hidden.shape[2]
    held_count = held_hidden.shape[2]
    text_slots = text_kv.shape[2]

    index_row = jnp.zeros((request_count, 1, model_width), jnp.bfloat16)
    index_row = index_row.at[:, 0, :held_count].set(recompute_rows[0].astype(jnp.bfloat16))
    payload = jnp.concatenate([stale_kv[0], held_hidden[0], index_row], axis=1)
    arrivals = [rotated(payload, "patch", distance) for distance in range(1, patch_count)]

    full_qkv, full_out = gather_weights(w_qkv, w_out)
    head_width = full_out.shape[0]
    key_weights = full_qkv[:, head_width:]

    others = []
    for slot in range(request_count):
        mod_rows = modulation[0, slot]
        stale_rows = jnp.concatenate([arrival[slot, :patch_rows] for arrival in arrivals], axis=0)
        held_rows = jnp.concatenate(
            [arrival[slot, patch_rows : patch_rows + held_count] for arrival in arrivals], axis=0
        )
        redo_index = jnp.concatenate(
            [
                arrival[slot, patch_rows + held_count, :held_count].astype(jnp.int32)
                + number * patch_rows
                for number, arrival in enumerate(arrivals)
            ]
        )
        held_norm = modulate(held_rows, mod_rows[0], mod_rows[1])
        redone = jnp.dot(held_norm, key_weights, preferred_element_type=jnp.float32).astype(
            jnp.bfloat16
        )
        others.append(stale_rows.at[redo_index].set(redone))
    others = jnp.stack(others)

    def process(layer_input, slot_index):
        mod_rows = lax.dynamic_index_in_dim(modulation[0], slot_index, 0, keepdims=False)
        text_rows = lax.dynamic_index_in_dim(text_kv[0], slot_index, 0, keepdims=False)
        text_count = lax.dynamic_index_in_dim(text_lengths, slot_index, 0, keepdims=False)
        other_rows = lax.dynamic_index_in_dim(others, slot_index, 0, keepdims=False)
        normed = modulate(layer_input, mod_rows[0], mod_rows[1])
        projected = jnp.dot(normed, full_qkv, preferred_element_type=jnp.float32).astype(
            jnp.bfloat16
        )
        fresh_rows = projected[:, head_width:]
        context = jnp.concatenate([text_rows, fresh_rows, other_rows], axis=0)
        usable = jnp.concatenate(
            [
                jnp.arange(text_slots) < text_count,
                jnp.ones((context.shape[0] - text_slots,), jnp.bool_),
            ]
        )
        attended = attend(
            projected[:, :head_width], context[:, :head_width], context[:, head_width:], usable
        )
        update = jnp.dot(attended, full_out, preferred_element_type=jnp.float32)
        layer_out = (layer_input.astype(jnp.float32) + mod_rows[2] * update).astype(jnp.bfloat16)
        return layer_out, fresh_rows

    first_section = section_index == 0
    half_width = model_width // 2

    out_1, fresh_1 = process(hidden[0], 0)
    received_1 = shifted(out_1, "section", 1)
    input_2 = jnp.where(first_section, hidden[1], received_1)
    out_2, fresh_2 = process(input_2, jnp.where(first_section, 1, 0))
    returned_a = shifted(out_2[:, :half_width], "section", -1)
    received_2 = shifted(out_2, "section", 1)
    out_3, fresh_3 = process(received_2, 1)
    returned_b = shifted(out_3[:, :half_width], "section", -1)

    cache = jnp.stack(
        [jnp.where(first_section, fresh_1, fresh_2), jnp.where(first_section, fresh_2, fresh_3)]
    )
    last_out = jnp.stack([out_2, out_3])
    returned = jnp.stack([returned_a, returned_b])
    own_half = jnp.where(first_section, returned, last_out[:, :, half_width:])
    source_half = lax.dynamic_slice_in_dim(hidden, section_index * half_width, half_width, 2)
    latents = coefficients[:, 0][:, None, None] * source_half.astype(jnp.float32) + coefficients[
        :, 1
    ][:, None, None] * own_half.astype(jnp.float32)
    return (latents, cache[None])


def solution(mesh):
    return jax.shard_map(
        body,
        mesh=mesh,
        in_specs=(
            P("req", "patch", None),
            P("section", ("patch", "req"), None),
            P("section", ("patch", "req"), None),
            P("section", "req", None, None),
            P("section", "req", None, None),
            P("req"),
            P("section", "req", "patch", None),
            P("section", "req", "patch", None),
            P("section", "req", "patch"),
            P("req", None),
        ),
        out_specs=(P("req", "patch", "section"), P("section", "req", "patch", None)),
        check_vma=False,
    )
```

```python
import jax
import jax.numpy as jnp
from jax import lax
from jax.experimental import pallas as pl
from jax.experimental.pallas import tpu as pltpu
from jax.sharding import PartitionSpec as P

HEADS = 12


norm_eps = 1e-06
score_scale = 0.125


def shifted(block, axis, distance):
    devices = range(lax.axis_size(axis))
    route = [(i - distance, i) for i in devices if i - distance in devices]
    return lax.ppermute(block, axis, route)


def rotated(block, axis, distance):
    size = lax.axis_size(axis)
    return lax.ppermute(block, axis, [(i, (i + distance) % size) for i in range(size)])


def modulate(row_block, shift_row, scale_row):
    values = row_block.astype(jnp.float32)
    centre = values - jnp.mean(values, axis=-1, keepdims=True)
    spread = jnp.mean(centre * centre, axis=-1, keepdims=True)
    return (centre * lax.rsqrt(spread + norm_eps) * (1.0 + scale_row) + shift_row).astype(
        jnp.bfloat16
    )


def attend(queries, key_rows, value_rows, usable):
    row_count = queries.shape[0]
    feature_count = queries.shape[1]
    query_heads = queries.reshape(row_count, HEADS, feature_count // HEADS)
    key_heads = key_rows.reshape(key_rows.shape[0], HEADS, feature_count // HEADS)
    value_heads = value_rows.reshape(value_rows.shape[0], HEADS, feature_count // HEADS)
    scores = (
        jnp.einsum("qhd,khd->hqk", query_heads, key_heads, preferred_element_type=jnp.float32)
        * score_scale
    )
    scores = jnp.where(usable[None, None, :], scores, -1e30)
    row_max = jnp.max(scores, axis=-1, keepdims=True)
    exp_scores = jnp.exp(scores - row_max)
    soft_weights = (exp_scores / jnp.sum(exp_scores, axis=-1, keepdims=True)).astype(jnp.bfloat16)
    attended = jnp.einsum(
        "hqk,khd->qhd", soft_weights, value_heads, preferred_element_type=jnp.float32
    )
    return attended.reshape(row_count, feature_count).astype(jnp.bfloat16)


def attention_kernel(count_ref, q_ref, fk_ref, fv_ref, tk_ref, tv_ref, ok_ref, ov_ref, out_ref):
    text_count = count_ref[0]
    lanes = q_ref.shape[1]
    half = lanes // 2
    queries = q_ref[...]
    lane = lax.broadcasted_iota(jnp.int32, queries.shape, 1)
    text_slot = lax.broadcasted_iota(jnp.int32, (queries.shape[0], tk_ref.shape[0]), 1)
    blocks = ((tk_ref, tv_ref), (fk_ref, fv_ref), (ok_ref, ov_ref))
    result = jnp.zeros(out_ref.shape, jnp.float32)
    for head in range(2):
        own = (lane >= half) if head else (lane < half)
        masked = jnp.where(own, queries, jnp.zeros_like(queries))
        scores = []
        for number, (key_ref, _) in enumerate(blocks):
            s = lax.dot_general(
                masked, key_ref[...], (((1,), (1,)), ((), ())), preferred_element_type=jnp.float32
            ) * score_scale
            if number == 0:
                s = jnp.where(text_slot < text_count, s, -1e30)
            scores.append(s)
        row_max = scores[0].max(axis=1, keepdims=True)
        for s in scores[1:]:
            row_max = jnp.maximum(row_max, s.max(axis=1, keepdims=True))
        exps = [jnp.exp(s - row_max) for s in scores]
        total = exps[0].sum(axis=1, keepdims=True)
        for e in exps[1:]:
            total = total + e.sum(axis=1, keepdims=True)
        part = jnp.zeros(out_ref.shape, jnp.float32)
        for e, (_, value_ref) in zip(exps, blocks):
            weights = (e / total).astype(jnp.bfloat16)
            part = part + jnp.dot(weights, value_ref[...], preferred_element_type=jnp.float32)
        result = jnp.where(own, part, result)
    out_ref[...] = result.astype(out_ref.dtype)


def fused_attention(projected, text_rows, other_rows, text_count):
    rows = projected.shape[0]
    width = text_rows.shape[1] // 2
    pairs = width // 128
    text_slots = text_rows.shape[0]
    other_count = other_rows.shape[0]

    def col(offset, height):
        return pl.BlockSpec((height, 128), lambda j, c: (0, j + offset))

    grid_spec = pltpu.PrefetchScalarGridSpec(
        num_scalar_prefetch=1,
        grid=(pairs,),
        in_specs=[
            col(0, rows),
            col(pairs, rows),
            col(2 * pairs, rows),
            col(0, text_slots),
            col(pairs, text_slots),
            col(0, other_count),
            col(pairs, other_count),
        ],
        out_specs=col(0, rows),
    )
    keys = text_slots + rows + other_count
    return pl.pallas_call(
        attention_kernel,
        grid_spec=grid_spec,
        out_shape=jax.ShapeDtypeStruct((rows, width), jnp.bfloat16),
        cost_estimate=pl.CostEstimate(
            flops=4 * rows * keys * width * 2,
            transcendentals=rows * keys * HEADS,
            bytes_accessed=2 * (rows * 3 * width + keys * 2 * width),
        ),
    )(text_count.reshape(1), projected, projected, projected, text_rows, text_rows, other_rows, other_rows)


def gather_weights(w_qkv, w_out):
    qkv_shard = w_qkv[0]
    out_shard = w_out[0]
    qkv_rows, qkv_cols = qkv_shard.shape
    out_rows, out_cols = out_shard.shape
    out_folded = out_shard.reshape(-1, qkv_cols)
    chunk = jnp.concatenate([qkv_shard, out_folded], axis=0)
    chunk_rows = chunk.shape[0]
    gathered = lax.all_gather(chunk, "patch", axis=0, tiled=True)
    gathered = lax.all_gather(gathered, "req", axis=0, tiled=True)
    patches = lax.axis_size("patch")
    requests = lax.axis_size("req")
    blocks = gathered.reshape(requests, patches, chunk_rows, qkv_cols)
    full_out = (
        blocks[:, :, qkv_rows:].transpose(1, 0, 2, 3).reshape(patches * requests, -1)
    ).reshape(-1, out_cols)
    return gathered, full_out


def spread_columns(values, patches, requests, chunk_rows):
    count = values.shape[0]
    values = values.reshape(count, patches, requests, -1).transpose(0, 2, 1, 3)
    pad = chunk_rows - values.shape[3]
    values = jnp.pad(values, ((0, 0), (0, 0), (0, 0), (0, pad)))
    return values.reshape(count, -1)


def body(
    hidden,
    w_qkv,
    w_out,
    modulation,
    text_kv,
    text_lengths,
    stale_kv,
    held_hidden,
    recompute_rows,
    coefficients,
):
    section_index = lax.axis_index("section")
    patch_count = lax.axis_size("patch")
    request_count = hidden.shape[0]
    patch_rows = hidden.shape[1]
    model_width = hidden.shape[2]
    held_count = held_hidden.shape[2]
    text_slots = text_kv.shape[2]

    index_row = jnp.zeros((request_count, 1, model_width), jnp.bfloat16)
    index_row = index_row.at[:, 0, :held_count].set(recompute_rows[0].astype(jnp.bfloat16))
    payload = jnp.concatenate([stale_kv[0], held_hidden[0], index_row], axis=1)
    arrivals = [rotated(payload, "patch", distance) for distance in range(1, patch_count)]

    full_qkv, full_out = gather_weights(w_qkv, w_out)
    head_width = full_out.shape[0]
    key_weights = full_qkv[:, head_width:]
    patches = lax.axis_size("patch")
    requests = lax.axis_size("req")
    chunk_rows = full_qkv.shape[0] // (patches * requests)

    def spread(values):
        return spread_columns(values, patches, requests, chunk_rows)

    others = []
    for slot in range(request_count):
        mod_rows = modulation[0, slot]
        stale_rows = jnp.concatenate([arrival[slot, :patch_rows] for arrival in arrivals], axis=0)
        held_rows = jnp.concatenate(
            [arrival[slot, patch_rows : patch_rows + held_count] for arrival in arrivals], axis=0
        )
        redo_index = jnp.concatenate(
            [
                arrival[slot, patch_rows + held_count, :held_count].astype(jnp.int32)
                + number * patch_rows
                for number, arrival in enumerate(arrivals)
            ]
        )
        held_norm = modulate(held_rows, mod_rows[0], mod_rows[1])
        redone = jnp.dot(spread(held_norm), key_weights, preferred_element_type=jnp.float32).astype(
            jnp.bfloat16
        )
        others.append(stale_rows.at[redo_index].set(redone))
    others = jnp.stack(others)

    def process(layer_input, slot_index):
        mod_rows = lax.dynamic_index_in_dim(modulation[0], slot_index, 0, keepdims=False)
        text_rows = lax.dynamic_index_in_dim(text_kv[0], slot_index, 0, keepdims=False)
        text_count = lax.dynamic_index_in_dim(text_lengths, slot_index, 0, keepdims=False)
        other_rows = lax.dynamic_index_in_dim(others, slot_index, 0, keepdims=False)
        normed = modulate(layer_input, mod_rows[0], mod_rows[1])
        projected = jnp.dot(spread(normed), full_qkv, preferred_element_type=jnp.float32).astype(
            jnp.bfloat16
        )
        fresh_rows = projected[:, head_width:]
        attended = fused_attention(projected, text_rows, other_rows, text_count)
        update = jnp.dot(attended, full_out, preferred_element_type=jnp.float32)
        layer_out = (layer_input.astype(jnp.float32) + mod_rows[2] * update).astype(jnp.bfloat16)
        return layer_out, fresh_rows

    first_section = section_index == 0
    half_width = model_width // 2

    out_1, fresh_1 = process(hidden[0], 0)
    received_1 = shifted(out_1, "section", 1)
    input_2 = jnp.where(first_section, hidden[1], received_1)
    out_2, fresh_2 = process(input_2, jnp.where(first_section, 1, 0))
    returned_a = shifted(out_2[:, :half_width], "section", -1)
    received_2 = shifted(out_2, "section", 1)
    out_3, fresh_3 = process(received_2, 1)
    returned_b = shifted(out_3[:, :half_width], "section", -1)

    cache = jnp.stack(
        [jnp.where(first_section, fresh_1, fresh_2), jnp.where(first_section, fresh_2, fresh_3)]
    )
    last_out = jnp.stack([out_2, out_3])
    returned = jnp.stack([returned_a, returned_b])
    own_half = jnp.where(first_section, returned, last_out[:, :, half_width:])
    source_half = lax.dynamic_slice_in_dim(hidden, section_index * half_width, half_width, 2)
    latents = coefficients[:, 0][:, None, None] * source_half.astype(jnp.float32) + coefficients[
        :, 1
    ][:, None, None] * own_half.astype(jnp.float32)
    return (latents, cache[None])


def solution(mesh):
    return jax.shard_map(
        body,
        mesh=mesh,
        in_specs=(
            P("req", "patch", None),
            P("section", ("patch", "req"), None),
            P("section", ("patch", "req"), None),
            P("section", "req", None, None),
            P("section", "req", None, None),
            P("req"),
            P("section", "req", "patch", None),
            P("section", "req", "patch", None),
            P("section", "req", "patch"),
            P("req", None),
        ),
        out_specs=(P("req", "patch", "section"), P("section", "req", "patch", None)),
        check_vma=False,
    )
```

```python
import jax
import jax.numpy as jnp
from jax import lax
from jax.experimental import pallas as pl
from jax.experimental.pallas import tpu as pltpu
from jax.sharding import PartitionSpec as P

HEADS = 12


norm_eps = 1e-06
score_scale = 0.125


def shifted(block, axis, distance):
    devices = range(lax.axis_size(axis))
    route = [(i - distance, i) for i in devices if i - distance in devices]
    return lax.ppermute(block, axis, route)


def rotated(block, axis, distance):
    size = lax.axis_size(axis)
    return lax.ppermute(block, axis, [(i, (i + distance) % size) for i in range(size)])


def modulate(row_block, shift_row, scale_row):
    values = row_block.astype(jnp.float32)
    centre = values - jnp.mean(values, axis=-1, keepdims=True)
    spread = jnp.mean(centre * centre, axis=-1, keepdims=True)
    return (centre * lax.rsqrt(spread + norm_eps) * (1.0 + scale_row) + shift_row).astype(
        jnp.bfloat16
    )


def attend(queries, key_rows, value_rows, usable):
    row_count = queries.shape[0]
    feature_count = queries.shape[1]
    query_heads = queries.reshape(row_count, HEADS, feature_count // HEADS)
    key_heads = key_rows.reshape(key_rows.shape[0], HEADS, feature_count // HEADS)
    value_heads = value_rows.reshape(value_rows.shape[0], HEADS, feature_count // HEADS)
    scores = (
        jnp.einsum("qhd,khd->hqk", query_heads, key_heads, preferred_element_type=jnp.float32)
        * score_scale
    )
    scores = jnp.where(usable[None, None, :], scores, -1e30)
    row_max = jnp.max(scores, axis=-1, keepdims=True)
    exp_scores = jnp.exp(scores - row_max)
    soft_weights = (exp_scores / jnp.sum(exp_scores, axis=-1, keepdims=True)).astype(jnp.bfloat16)
    attended = jnp.einsum(
        "hqk,khd->qhd", soft_weights, value_heads, preferred_element_type=jnp.float32
    )
    return attended.reshape(row_count, feature_count).astype(jnp.bfloat16)


def attention_kernel(
    count_ref, q_ref, fk_ref, fv_ref, tk_ref, tv_ref, ok_ref, ov_ref, keep_ref, rk_ref, rv_ref, out_ref
):
    text_count = count_ref[0]
    lanes = q_ref.shape[1]
    half = lanes // 2
    queries = q_ref[...]
    lane = lax.broadcasted_iota(jnp.int32, queries.shape, 1)
    text_slot = lax.broadcasted_iota(jnp.int32, (queries.shape[0], tk_ref.shape[0]), 1)
    other_kept = keep_ref[...] > 0
    blocks = ((tk_ref, tv_ref), (fk_ref, fv_ref), (ok_ref, ov_ref), (rk_ref, rv_ref))
    result = jnp.zeros(out_ref.shape, jnp.float32)
    for head in range(2):
        own = (lane >= half) if head else (lane < half)
        masked = jnp.where(own, queries, jnp.zeros_like(queries))
        scores = []
        for number, (key_ref, _) in enumerate(blocks):
            s = lax.dot_general(
                masked, key_ref[...], (((1,), (1,)), ((), ())), preferred_element_type=jnp.float32
            ) * score_scale
            if number == 0:
                s = jnp.where(text_slot < text_count, s, -1e30)
            if number == 2:
                s = jnp.where(other_kept, s, -1e30)
            scores.append(s)
        row_max = scores[0].max(axis=1, keepdims=True)
        for s in scores[1:]:
            row_max = jnp.maximum(row_max, s.max(axis=1, keepdims=True))
        exps = [jnp.exp(s - row_max) for s in scores]
        total = exps[0].sum(axis=1, keepdims=True)
        for e in exps[1:]:
            total = total + e.sum(axis=1, keepdims=True)
        inverse = 1.0 / total
        part = jnp.zeros(out_ref.shape, jnp.float32)
        for e, (_, value_ref) in zip(exps, blocks):
            weights = (e * inverse).astype(jnp.bfloat16)
            part = part + jnp.dot(weights, value_ref[...], preferred_element_type=jnp.float32)
        result = jnp.where(own, part, result)
    out_ref[...] = result.astype(out_ref.dtype)


def fused_attention(projected, text_rows, other_rows, other_keep, redone_rows, text_count):
    rows = projected.shape[0]
    width = text_rows.shape[1] // 2
    pairs = width // 128
    text_slots = text_rows.shape[0]
    other_count = other_rows.shape[0]
    redone_count = redone_rows.shape[0]

    def col(offset, height):
        return pl.BlockSpec((height, 128), lambda j, c: (0, j + offset))

    grid_spec = pltpu.PrefetchScalarGridSpec(
        num_scalar_prefetch=1,
        grid=(pairs,),
        in_specs=[
            col(0, rows),
            col(pairs, rows),
            col(2 * pairs, rows),
            col(0, text_slots),
            col(pairs, text_slots),
            col(0, other_count),
            col(pairs, other_count),
            pl.BlockSpec((1, other_count), lambda j, c: (0, 0)),
            col(0, redone_count),
            col(pairs, redone_count),
        ],
        out_specs=col(0, rows),
    )
    keys = text_slots + rows + other_count + redone_count
    return pl.pallas_call(
        attention_kernel,
        grid_spec=grid_spec,
        out_shape=jax.ShapeDtypeStruct((rows, width), jnp.bfloat16),
        cost_estimate=pl.CostEstimate(
            flops=4 * rows * keys * width * 2,
            transcendentals=rows * keys * HEADS,
            bytes_accessed=2 * (rows * 3 * width + keys * 2 * width),
        ),
    )(
        text_count.reshape(1),
        projected,
        projected,
        projected,
        text_rows,
        text_rows,
        other_rows,
        other_rows,
        other_keep,
        redone_rows,
        redone_rows,
    )


def gather_weights(w_qkv, w_out):
    qkv_shard = w_qkv[0]
    out_shard = w_out[0]
    qkv_rows, qkv_cols = qkv_shard.shape
    out_rows, out_cols = out_shard.shape
    out_folded = out_shard.reshape(-1, qkv_cols)
    chunk = jnp.concatenate([qkv_shard, out_folded], axis=0)
    chunk_rows = chunk.shape[0]
    gathered = lax.all_gather(chunk, "patch", axis=0, tiled=True)
    gathered = lax.all_gather(gathered, "req", axis=0, tiled=True)
    patches = lax.axis_size("patch")
    requests = lax.axis_size("req")
    blocks = gathered.reshape(requests, patches, chunk_rows, qkv_cols)
    full_out = (
        blocks[:, :, qkv_rows:].transpose(1, 0, 2, 3).reshape(patches * requests, -1)
    ).reshape(-1, out_cols)
    return gathered, full_out


def spread_columns(values, patches, requests, chunk_rows):
    count = values.shape[0]
    values = values.reshape(count, patches, requests, -1).transpose(0, 2, 1, 3)
    pad = chunk_rows - values.shape[3]
    values = jnp.pad(values, ((0, 0), (0, 0), (0, 0), (0, pad)))
    return values.reshape(count, -1)


def body(
    hidden,
    w_qkv,
    w_out,
    modulation,
    text_kv,
    text_lengths,
    stale_kv,
    held_hidden,
    recompute_rows,
    coefficients,
):
    section_index = lax.axis_index("section")
    patch_count = lax.axis_size("patch")
    request_count = hidden.shape[0]
    patch_rows = hidden.shape[1]
    model_width = hidden.shape[2]
    held_count = held_hidden.shape[2]
    text_slots = text_kv.shape[2]

    index_row = jnp.zeros((request_count, 1, model_width), jnp.bfloat16)
    index_row = index_row.at[:, 0, :held_count].set(recompute_rows[0].astype(jnp.bfloat16))
    payload = jnp.concatenate([stale_kv[0], held_hidden[0], index_row], axis=1)
    arrivals = [rotated(payload, "patch", distance) for distance in range(1, patch_count)]

    full_qkv, full_out = gather_weights(w_qkv, w_out)
    head_width = full_out.shape[0]
    key_weights = full_qkv[:, head_width:]
    patches = lax.axis_size("patch")
    requests = lax.axis_size("req")
    chunk_rows = full_qkv.shape[0] // (patches * requests)

    def spread(values):
        return spread_columns(values, patches, requests, chunk_rows)

    others, keeps, redones = [], [], []
    for slot in range(request_count):
        mod_rows = modulation[0, slot]
        stale_rows = jnp.concatenate([arrival[slot, :patch_rows] for arrival in arrivals], axis=0)
        held_rows = jnp.concatenate(
            [arrival[slot, patch_rows : patch_rows + held_count] for arrival in arrivals], axis=0
        )
        redo_index = jnp.concatenate(
            [
                arrival[slot, patch_rows + held_count, :held_count].astype(jnp.int32)
                + number * patch_rows
                for number, arrival in enumerate(arrivals)
            ]
        )
        replaced = jnp.any(
            redo_index[:, None] == jnp.arange(stale_rows.shape[0])[None, :], axis=0
        )
        held_norm = modulate(held_rows, mod_rows[0], mod_rows[1])
        redone = jnp.dot(spread(held_norm), key_weights, preferred_element_type=jnp.float32).astype(
            jnp.bfloat16
        )
        others.append(stale_rows)
        keeps.append(jnp.where(replaced, 0, 1).astype(jnp.int32)[None, :])
        redones.append(redone)
    others = jnp.stack(others)
    keeps = jnp.stack(keeps)
    redones = jnp.stack(redones)

    def process(layer_input, slot_index):
        mod_rows = lax.dynamic_index_in_dim(modulation[0], slot_index, 0, keepdims=False)
        text_rows = lax.dynamic_index_in_dim(text_kv[0], slot_index, 0, keepdims=False)
        text_count = lax.dynamic_index_in_dim(text_lengths, slot_index, 0, keepdims=False)
        other_rows = lax.dynamic_index_in_dim(others, slot_index, 0, keepdims=False)
        other_keep = lax.dynamic_index_in_dim(keeps, slot_index, 0, keepdims=False)
        redone_rows = lax.dynamic_index_in_dim(redones, slot_index, 0, keepdims=False)
        normed = modulate(layer_input, mod_rows[0], mod_rows[1])
        projected = jnp.dot(spread(normed), full_qkv, preferred_element_type=jnp.float32).astype(
            jnp.bfloat16
        )
        fresh_rows = projected[:, head_width:]
        attended = fused_attention(
            projected, text_rows, other_rows, other_keep, redone_rows, text_count
        )
        update = jnp.dot(attended, full_out, preferred_element_type=jnp.float32)
        layer_out = (layer_input.astype(jnp.float32) + mod_rows[2] * update).astype(jnp.bfloat16)
        return layer_out, fresh_rows

    first_section = section_index == 0
    half_width = model_width // 2

    out_1, fresh_1 = process(hidden[0], 0)
    received_1 = shifted(out_1, "section", 1)
    input_2 = jnp.where(first_section, hidden[1], received_1)
    out_2, fresh_2 = process(input_2, jnp.where(first_section, 1, 0))
    returned_a = shifted(out_2[:, :half_width], "section", -1)
    received_2 = shifted(out_2, "section", 1)
    out_3, fresh_3 = process(received_2, 1)
    returned_b = shifted(out_3[:, :half_width], "section", -1)

    cache = jnp.stack(
        [jnp.where(first_section, fresh_1, fresh_2), jnp.where(first_section, fresh_2, fresh_3)]
    )
    last_out = jnp.stack([out_2, out_3])
    returned = jnp.stack([returned_a, returned_b])
    own_half = jnp.where(first_section, returned, last_out[:, :, half_width:])
    source_half = lax.dynamic_slice_in_dim(hidden, section_index * half_width, half_width, 2)
    latents = coefficients[:, 0][:, None, None] * source_half.astype(jnp.float32) + coefficients[
        :, 1
    ][:, None, None] * own_half.astype(jnp.float32)
    return (latents, cache[None])


def solution(mesh):
    return jax.shard_map(
        body,
        mesh=mesh,
        in_specs=(
            P("req", "patch", None),
            P("section", ("patch", "req"), None),
            P("section", ("patch", "req"), None),
            P("section", "req", None, None),
            P("section", "req", None, None),
            P("req"),
            P("section", "req", "patch", None),
            P("section", "req", "patch", None),
            P("section", "req", "patch"),
            P("req", None),
        ),
        out_specs=(P("req", "patch", "section"), P("section", "req", "patch", None)),
        check_vma=False,
    )
```

```python
import jax
import jax.numpy as jnp
from jax import lax
from jax.experimental import pallas as pl
from jax.experimental.pallas import tpu as pltpu
from jax.sharding import PartitionSpec as P

HEADS = 12


norm_eps = 1e-06
score_scale = 0.125


def shifted(block, axis, distance):
    devices = range(lax.axis_size(axis))
    route = [(i - distance, i) for i in devices if i - distance in devices]
    return lax.ppermute(block, axis, route)


def rotated(block, axis, distance):
    size = lax.axis_size(axis)
    return lax.ppermute(block, axis, [(i, (i + distance) % size) for i in range(size)])


def modulate(row_block, shift_row, scale_row):
    values = row_block.astype(jnp.float32)
    centre = values - jnp.mean(values, axis=-1, keepdims=True)
    spread = jnp.mean(centre * centre, axis=-1, keepdims=True)
    return (centre * lax.rsqrt(spread + norm_eps) * (1.0 + scale_row) + shift_row).astype(
        jnp.bfloat16
    )


def attend(queries, key_rows, value_rows, usable):
    row_count = queries.shape[0]
    feature_count = queries.shape[1]
    query_heads = queries.reshape(row_count, HEADS, feature_count // HEADS)
    key_heads = key_rows.reshape(key_rows.shape[0], HEADS, feature_count // HEADS)
    value_heads = value_rows.reshape(value_rows.shape[0], HEADS, feature_count // HEADS)
    scores = (
        jnp.einsum("qhd,khd->hqk", query_heads, key_heads, preferred_element_type=jnp.float32)
        * score_scale
    )
    scores = jnp.where(usable[None, None, :], scores, -1e30)
    row_max = jnp.max(scores, axis=-1, keepdims=True)
    exp_scores = jnp.exp(scores - row_max)
    soft_weights = (exp_scores / jnp.sum(exp_scores, axis=-1, keepdims=True)).astype(jnp.bfloat16)
    attended = jnp.einsum(
        "hqk,khd->qhd", soft_weights, value_heads, preferred_element_type=jnp.float32
    )
    return attended.reshape(row_count, feature_count).astype(jnp.bfloat16)


def attention_kernel(count_ref, q_ref, fk_ref, fv_ref, tk_ref, tv_ref, *refs):
    *other_refs, keep_ref, rk_ref, rv_ref, out_ref = refs
    text_count = count_ref[0]
    lanes = q_ref.shape[1]
    half = lanes // 2
    queries = q_ref[...]
    lane = lax.broadcasted_iota(jnp.int32, queries.shape, 1)
    text_slot = lax.broadcasted_iota(jnp.int32, (queries.shape[0], tk_ref.shape[0]), 1)
    kept = keep_ref[...] > 0
    other_rows = other_refs[0].shape[0]
    blocks = [(tk_ref, tv_ref, "text"), (fk_ref, fv_ref, None)]
    for number in range(len(other_refs) // 2):
        blocks.append((other_refs[2 * number], other_refs[2 * number + 1], number))
    blocks.append((rk_ref, rv_ref, None))
    result = jnp.zeros(out_ref.shape, jnp.float32)
    for head in range(2):
        own = (lane >= half) if head else (lane < half)
        masked = jnp.where(own, queries, jnp.zeros_like(queries))
        scores = []
        for key_ref, _, mask in blocks:
            s = lax.dot_general(
                masked, key_ref[...], (((1,), (1,)), ((), ())), preferred_element_type=jnp.float32
            ) * score_scale
            if mask == "text":
                s = jnp.where(text_slot < text_count, s, -1e30)
            elif mask is not None:
                s = jnp.where(kept[:, mask * other_rows : (mask + 1) * other_rows], s, -1e30)
            scores.append(s)
        row_max = scores[0].max(axis=1, keepdims=True)
        for s in scores[1:]:
            row_max = jnp.maximum(row_max, s.max(axis=1, keepdims=True))
        exps = [jnp.exp(s - row_max) for s in scores]
        total = exps[0].sum(axis=1, keepdims=True)
        for e in exps[1:]:
            total = total + e.sum(axis=1, keepdims=True)
        inverse = 1.0 / total
        part = jnp.zeros(out_ref.shape, jnp.float32)
        for e, (_, value_ref, _) in zip(exps, blocks):
            weights = (e * inverse).astype(jnp.bfloat16)
            part = part + jnp.dot(weights, value_ref[...], preferred_element_type=jnp.float32)
        result = jnp.where(own, part, result)
    out_ref[...] = result.astype(out_ref.dtype)


def fused_attention(projected, text_all, arrivals, keep_all, redone_all, text_count, slot, patch_rows):
    rows = projected.shape[0]
    width = text_all.shape[2] // 2
    pairs = width // 128
    text_slots = text_all.shape[1]
    keep_width = keep_all.shape[2]
    redone_count = redone_all.shape[1]

    def col(offset, height):
        return pl.BlockSpec((height, 128), lambda j, c: (0, j + offset))

    def slotted(offset, height):
        return pl.BlockSpec((None, height, 128), lambda j, c: (c[1], 0, j + offset))

    arrival_specs = []
    for _ in arrivals:
        arrival_specs += [slotted(0, patch_rows), slotted(pairs, patch_rows)]
    grid_spec = pltpu.PrefetchScalarGridSpec(
        num_scalar_prefetch=1,
        grid=(pairs,),
        in_specs=[
            col(0, rows),
            col(pairs, rows),
            col(2 * pairs, rows),
            slotted(0, text_slots),
            slotted(pairs, text_slots),
            *arrival_specs,
            pl.BlockSpec((None, 1, keep_width), lambda j, c: (c[1], 0, 0)),
            slotted(0, redone_count),
            slotted(pairs, redone_count),
        ],
        out_specs=col(0, rows),
    )
    keys = text_slots + rows + keep_width + redone_count
    arrival_args = []
    for arrival in arrivals:
        arrival_args += [arrival, arrival]
    scalars = jnp.stack([text_count, slot]).astype(jnp.int32)
    return pl.pallas_call(
        attention_kernel,
        grid_spec=grid_spec,
        out_shape=jax.ShapeDtypeStruct((rows, width), jnp.bfloat16),
        cost_estimate=pl.CostEstimate(
            flops=4 * rows * keys * width * 2,
            transcendentals=rows * keys * HEADS,
            bytes_accessed=2 * (rows * 3 * width + keys * 2 * width),
        ),
    )(
        scalars,
        projected,
        projected,
        projected,
        text_all,
        text_all,
        *arrival_args,
        keep_all,
        redone_all,
        redone_all,
    )


def gather_weights(w_qkv, w_out):
    qkv_shard = w_qkv[0]
    out_shard = w_out[0]
    qkv_rows, qkv_cols = qkv_shard.shape
    out_rows, out_cols = out_shard.shape
    out_folded = out_shard.reshape(-1, qkv_cols)
    chunk = jnp.concatenate([qkv_shard, out_folded], axis=0)
    chunk_rows = chunk.shape[0]
    gathered = lax.all_gather(chunk, "patch", axis=0, tiled=True)
    gathered = lax.all_gather(gathered, "req", axis=0, tiled=True)
    patches = lax.axis_size("patch")
    requests = lax.axis_size("req")
    blocks = gathered.reshape(requests, patches, chunk_rows, qkv_cols)
    full_out = (
        blocks[:, :, qkv_rows:].transpose(1, 0, 2, 3).reshape(patches * requests, -1)
    ).reshape(-1, out_cols)
    return gathered, full_out


def spread_columns(values, patches, requests, chunk_rows):
    count = values.shape[0]
    values = values.reshape(count, patches, requests, -1).transpose(0, 2, 1, 3)
    pad = chunk_rows - values.shape[3]
    values = jnp.pad(values, ((0, 0), (0, 0), (0, 0), (0, pad)))
    return values.reshape(count, -1)


def body(
    hidden,
    w_qkv,
    w_out,
    modulation,
    text_kv,
    text_lengths,
    stale_kv,
    held_hidden,
    recompute_rows,
    coefficients,
):
    section_index = lax.axis_index("section")
    patch_count = lax.axis_size("patch")
    request_count = hidden.shape[0]
    patch_rows = hidden.shape[1]
    model_width = hidden.shape[2]
    held_count = held_hidden.shape[2]
    text_slots = text_kv.shape[2]

    index_row = jnp.zeros((request_count, 1, model_width), jnp.bfloat16)
    index_row = index_row.at[:, 0, :held_count].set(recompute_rows[0].astype(jnp.bfloat16))
    payload = jnp.concatenate([stale_kv[0], held_hidden[0], index_row], axis=1)
    arrivals = [rotated(payload, "patch", distance) for distance in range(1, patch_count)]

    full_qkv, full_out = gather_weights(w_qkv, w_out)
    head_width = full_out.shape[0]
    key_weights = full_qkv[:, head_width:]
    patches = lax.axis_size("patch")
    requests = lax.axis_size("req")
    chunk_rows = full_qkv.shape[0] // (patches * requests)

    def spread(values):
        return spread_columns(values, patches, requests, chunk_rows)

    keeps, redones = [], []
    for slot in range(request_count):
        mod_rows = modulation[0, slot]
        held_rows = jnp.concatenate(
            [arrival[slot, patch_rows : patch_rows + held_count] for arrival in arrivals], axis=0
        )
        redo_index = jnp.concatenate(
            [
                arrival[slot, patch_rows + held_count, :held_count].astype(jnp.int32)
                + number * patch_rows
                for number, arrival in enumerate(arrivals)
            ]
        )
        replaced = jnp.any(
            redo_index[:, None] == jnp.arange(len(arrivals) * patch_rows)[None, :], axis=0
        )
        held_norm = modulate(held_rows, mod_rows[0], mod_rows[1])
        redone = jnp.dot(spread(held_norm), key_weights, preferred_element_type=jnp.float32).astype(
            jnp.bfloat16
        )
        keeps.append(jnp.where(replaced, 0, 1).astype(jnp.int32)[None, :])
        redones.append(redone)
    keeps = jnp.stack(keeps)
    redones = jnp.stack(redones)

    def process(layer_input, slot_index):
        mod_rows = lax.dynamic_index_in_dim(modulation[0], slot_index, 0, keepdims=False)
        text_count = lax.dynamic_index_in_dim(text_lengths, slot_index, 0, keepdims=False)
        normed = modulate(layer_input, mod_rows[0], mod_rows[1])
        projected = jnp.dot(spread(normed), full_qkv, preferred_element_type=jnp.float32).astype(
            jnp.bfloat16
        )
        fresh_rows = projected[:, head_width:]
        attended = fused_attention(
            projected, text_kv[0], arrivals, keeps, redones, text_count, slot_index, patch_rows
        )
        update = jnp.dot(attended, full_out, preferred_element_type=jnp.float32)
        layer_out = (layer_input.astype(jnp.float32) + mod_rows[2] * update).astype(jnp.bfloat16)
        return layer_out, fresh_rows

    first_section = section_index == 0
    half_width = model_width // 2

    out_1, fresh_1 = process(hidden[0], jnp.int32(0))
    received_1 = shifted(out_1, "section", 1)
    input_2 = jnp.where(first_section, hidden[1], received_1)
    out_2, fresh_2 = process(input_2, jnp.where(first_section, 1, 0).astype(jnp.int32))
    returned_a = shifted(out_2[:, :half_width], "section", -1)
    received_2 = shifted(out_2, "section", 1)
    out_3, fresh_3 = process(received_2, jnp.int32(1))
    returned_b = shifted(out_3[:, :half_width], "section", -1)

    cache = jnp.stack(
        [jnp.where(first_section, fresh_1, fresh_2), jnp.where(first_section, fresh_2, fresh_3)]
    )
    last_out = jnp.stack([out_2, out_3])
    returned = jnp.stack([returned_a, returned_b])
    own_half = jnp.where(first_section, returned, last_out[:, :, half_width:])
    source_half = lax.dynamic_slice_in_dim(hidden, section_index * half_width, half_width, 2)
    latents = coefficients[:, 0][:, None, None] * source_half.astype(jnp.float32) + coefficients[
        :, 1
    ][:, None, None] * own_half.astype(jnp.float32)
    return (latents, cache[None])


def solution(mesh):
    return jax.shard_map(
        body,
        mesh=mesh,
        in_specs=(
            P("req", "patch", None),
            P("section", ("patch", "req"), None),
            P("section", ("patch", "req"), None),
            P("section", "req", None, None),
            P("section", "req", None, None),
            P("req"),
            P("section", "req", "patch", None),
            P("section", "req", "patch", None),
            P("section", "req", "patch"),
            P("req", None),
        ),
        out_specs=(P("req", "patch", "section"), P("section", "req", "patch", None)),
        check_vma=False,
    )
```

```python
import jax
import jax.numpy as jnp
from jax import lax
from jax.experimental import pallas as pl
from jax.experimental.pallas import tpu as pltpu
from jax.sharding import PartitionSpec as P

HEADS = 12


norm_eps = 1e-06
score_scale = 0.125


def shifted(block, axis, distance):
    devices = range(lax.axis_size(axis))
    route = [(i - distance, i) for i in devices if i - distance in devices]
    return lax.ppermute(block, axis, route)


def rotated(block, axis, distance):
    size = lax.axis_size(axis)
    return lax.ppermute(block, axis, [(i, (i + distance) % size) for i in range(size)])


def modulate(row_block, shift_row, scale_row):
    values = row_block.astype(jnp.float32)
    centre = values - jnp.mean(values, axis=-1, keepdims=True)
    spread = jnp.mean(centre * centre, axis=-1, keepdims=True)
    return (centre * lax.rsqrt(spread + norm_eps) * (1.0 + scale_row) + shift_row).astype(
        jnp.bfloat16
    )


def attend(queries, key_rows, value_rows, usable):
    row_count = queries.shape[0]
    feature_count = queries.shape[1]
    query_heads = queries.reshape(row_count, HEADS, feature_count // HEADS)
    key_heads = key_rows.reshape(key_rows.shape[0], HEADS, feature_count // HEADS)
    value_heads = value_rows.reshape(value_rows.shape[0], HEADS, feature_count // HEADS)
    scores = (
        jnp.einsum("qhd,khd->hqk", query_heads, key_heads, preferred_element_type=jnp.float32)
        * score_scale
    )
    scores = jnp.where(usable[None, None, :], scores, -1e30)
    row_max = jnp.max(scores, axis=-1, keepdims=True)
    exp_scores = jnp.exp(scores - row_max)
    soft_weights = (exp_scores / jnp.sum(exp_scores, axis=-1, keepdims=True)).astype(jnp.bfloat16)
    attended = jnp.einsum(
        "hqk,khd->qhd", soft_weights, value_heads, preferred_element_type=jnp.float32
    )
    return attended.reshape(row_count, feature_count).astype(jnp.bfloat16)


def attention_kernel(count_ref, q_ref, fk_ref, fv_ref, tk_ref, tv_ref, *refs):
    *other_refs, keep_ref, rk_ref, rv_ref, out_ref = refs
    text_count = count_ref[0]
    lanes = q_ref.shape[1]
    half = lanes // 2
    queries = q_ref[...] * jnp.asarray(score_scale, q_ref.dtype)
    lane = lax.broadcasted_iota(jnp.int32, queries.shape, 1)
    text_slot = lax.broadcasted_iota(jnp.int32, (queries.shape[0], tk_ref.shape[0]), 1)
    kept = keep_ref[...] > 0
    other_rows = other_refs[0].shape[0]
    blocks = [(tk_ref, tv_ref, "text"), (fk_ref, fv_ref, None)]
    for number in range(len(other_refs) // 2):
        blocks.append((other_refs[2 * number], other_refs[2 * number + 1], number))
    blocks.append((rk_ref, rv_ref, None))
    result = jnp.zeros(out_ref.shape, jnp.float32)
    for head in range(2):
        own = (lane >= half) if head else (lane < half)
        masked = jnp.where(own, queries, jnp.zeros_like(queries))
        scores = []
        for key_ref, _, mask in blocks:
            s = lax.dot_general(
                masked, key_ref[...], (((1,), (1,)), ((), ())), preferred_element_type=jnp.float32
            )
            if mask == "text":
                s = jnp.where(text_slot < text_count, s, -1e30)
            elif mask is not None:
                s = jnp.where(kept[:, mask * other_rows : (mask + 1) * other_rows], s, -1e30)
            scores.append(s)
        row_max = scores[0].max(axis=1, keepdims=True)
        for s in scores[1:]:
            row_max = jnp.maximum(row_max, s.max(axis=1, keepdims=True))
        exps = [jnp.exp(s - row_max) for s in scores]
        total = exps[0].sum(axis=1, keepdims=True)
        for e in exps[1:]:
            total = total + e.sum(axis=1, keepdims=True)
        inverse = 1.0 / total
        part = jnp.zeros(out_ref.shape, jnp.float32)
        for e, (_, value_ref, _) in zip(exps, blocks):
            weights = (e * inverse).astype(jnp.bfloat16)
            part = part + jnp.dot(weights, value_ref[...], preferred_element_type=jnp.float32)
        result = jnp.where(own, part, result)
    out_ref[...] = result.astype(out_ref.dtype)


def fused_attention(projected, text_all, arrivals, keep_all, redone_all, text_count, slot, patch_rows):
    rows = projected.shape[0]
    width = text_all.shape[2] // 2
    pairs = width // 128
    text_slots = text_all.shape[1]
    keep_width = keep_all.shape[2]
    redone_count = redone_all.shape[1]

    row_tile = rows // 2

    def col(offset, height):
        return pl.BlockSpec((height, 128), lambda j, i, c: (i, j + offset))

    def fixed(offset, height):
        return pl.BlockSpec((height, 128), lambda j, i, c: (0, j + offset))

    def slotted(offset, height):
        return pl.BlockSpec((None, height, 128), lambda j, i, c: (c[1], 0, j + offset))

    arrival_specs = []
    for _ in arrivals:
        arrival_specs += [slotted(0, patch_rows), slotted(pairs, patch_rows)]
    grid_spec = pltpu.PrefetchScalarGridSpec(
        num_scalar_prefetch=1,
        grid=(pairs, 2),
        in_specs=[
            col(0, row_tile),
            fixed(pairs, rows),
            fixed(2 * pairs, rows),
            slotted(0, text_slots),
            slotted(pairs, text_slots),
            *arrival_specs,
            pl.BlockSpec((None, 1, keep_width), lambda j, i, c: (c[1], 0, 0)),
            slotted(0, redone_count),
            slotted(pairs, redone_count),
        ],
        out_specs=col(0, row_tile),
    )
    keys = text_slots + rows + keep_width + redone_count
    arrival_args = []
    for arrival in arrivals:
        arrival_args += [arrival, arrival]
    scalars = jnp.stack([text_count, slot]).astype(jnp.int32)
    return pl.pallas_call(
        attention_kernel,
        grid_spec=grid_spec,
        out_shape=jax.ShapeDtypeStruct((rows, width), jnp.bfloat16),
        cost_estimate=pl.CostEstimate(
            flops=4 * rows * keys * width * 2,
            transcendentals=rows * keys * HEADS,
            bytes_accessed=2 * (rows * 3 * width + keys * 2 * width),
        ),
    )(
        scalars,
        projected,
        projected,
        projected,
        text_all,
        text_all,
        *arrival_args,
        keep_all,
        redone_all,
        redone_all,
    )


def gather_weights(w_qkv, w_out):
    qkv_shard = w_qkv[0]
    out_shard = w_out[0]
    qkv_rows, qkv_cols = qkv_shard.shape
    out_rows, out_cols = out_shard.shape
    out_folded = out_shard.reshape(-1, qkv_cols)
    chunk = jnp.concatenate([qkv_shard, out_folded], axis=0)
    chunk_rows = chunk.shape[0]
    gathered = lax.all_gather(chunk, "patch", axis=0, tiled=True)
    gathered = lax.all_gather(gathered, "req", axis=0, tiled=True)
    patches = lax.axis_size("patch")
    requests = lax.axis_size("req")
    blocks = gathered.reshape(requests, patches, chunk_rows, qkv_cols)
    full_out = (
        blocks[:, :, qkv_rows:].transpose(1, 0, 2, 3).reshape(patches * requests, -1)
    ).reshape(-1, out_cols)
    return gathered, full_out


def spread_columns(values, patches, requests, chunk_rows):
    count = values.shape[0]
    values = values.reshape(count, patches, requests, -1).transpose(0, 2, 1, 3)
    pad = chunk_rows - values.shape[3]
    values = jnp.pad(values, ((0, 0), (0, 0), (0, 0), (0, pad)))
    return values.reshape(count, -1)


def body(
    hidden,
    w_qkv,
    w_out,
    modulation,
    text_kv,
    text_lengths,
    stale_kv,
    held_hidden,
    recompute_rows,
    coefficients,
):
    section_index = lax.axis_index("section")
    patch_count = lax.axis_size("patch")
    request_count = hidden.shape[0]
    patch_rows = hidden.shape[1]
    model_width = hidden.shape[2]
    held_count = held_hidden.shape[2]
    text_slots = text_kv.shape[2]

    index_row = jnp.zeros((request_count, 1, model_width), jnp.bfloat16)
    index_row = index_row.at[:, 0, :held_count].set(recompute_rows[0].astype(jnp.bfloat16))
    payload = jnp.concatenate([stale_kv[0], held_hidden[0], index_row], axis=1)
    arrivals = [rotated(payload, "patch", distance) for distance in range(1, patch_count)]

    full_qkv, full_out = gather_weights(w_qkv, w_out)
    head_width = full_out.shape[0]
    key_weights = full_qkv[:, head_width:]
    patches = lax.axis_size("patch")
    requests = lax.axis_size("req")
    chunk_rows = full_qkv.shape[0] // (patches * requests)

    def spread(values):
        return spread_columns(values, patches, requests, chunk_rows)

    keeps, redones = [], []
    for slot in range(request_count):
        mod_rows = modulation[0, slot]
        held_rows = jnp.concatenate(
            [arrival[slot, patch_rows : patch_rows + held_count] for arrival in arrivals], axis=0
        )
        redo_index = jnp.concatenate(
            [
                arrival[slot, patch_rows + held_count, :held_count].astype(jnp.int32)
                + number * patch_rows
                for number, arrival in enumerate(arrivals)
            ]
        )
        replaced = jnp.any(
            redo_index[:, None] == jnp.arange(len(arrivals) * patch_rows)[None, :], axis=0
        )
        held_norm = modulate(held_rows, mod_rows[0], mod_rows[1])
        redone = jnp.dot(spread(held_norm), key_weights, preferred_element_type=jnp.float32).astype(
            jnp.bfloat16
        )
        keeps.append(jnp.where(replaced, 0, 1).astype(jnp.int32)[None, :])
        redones.append(redone)
    keeps = jnp.stack(keeps)
    redones = jnp.stack(redones)

    def process(layer_input, slot_index):
        mod_rows = lax.dynamic_index_in_dim(modulation[0], slot_index, 0, keepdims=False)
        text_count = lax.dynamic_index_in_dim(text_lengths, slot_index, 0, keepdims=False)
        normed = modulate(layer_input, mod_rows[0], mod_rows[1])
        projected = jnp.dot(spread(normed), full_qkv, preferred_element_type=jnp.float32).astype(
            jnp.bfloat16
        )
        fresh_rows = projected[:, head_width:]
        attended = fused_attention(
            projected, text_kv[0], arrivals, keeps, redones, text_count, slot_index, patch_rows
        )
        update = jnp.dot(attended, full_out, preferred_element_type=jnp.float32)
        layer_out = (layer_input.astype(jnp.float32) + mod_rows[2] * update).astype(jnp.bfloat16)
        return layer_out, fresh_rows

    first_section = section_index == 0
    half_width = model_width // 2

    out_1, fresh_1 = process(hidden[0], jnp.int32(0))
    received_1 = shifted(out_1, "section", 1)
    input_2 = jnp.where(first_section, hidden[1], received_1)
    out_2, fresh_2 = process(input_2, jnp.where(first_section, 1, 0).astype(jnp.int32))
    returned_a = shifted(out_2[:, :half_width], "section", -1)
    received_2 = shifted(out_2, "section", 1)
    out_3, fresh_3 = process(received_2, jnp.int32(1))
    returned_b = shifted(out_3[:, :half_width], "section", -1)

    cache = jnp.stack(
        [jnp.where(first_section, fresh_1, fresh_2), jnp.where(first_section, fresh_2, fresh_3)]
    )
    last_out = jnp.stack([out_2, out_3])
    returned = jnp.stack([returned_a, returned_b])
    own_half = jnp.where(first_section, returned, last_out[:, :, half_width:])
    source_half = lax.dynamic_slice_in_dim(hidden, section_index * half_width, half_width, 2)
    latents = coefficients[:, 0][:, None, None] * source_half.astype(jnp.float32) + coefficients[
        :, 1
    ][:, None, None] * own_half.astype(jnp.float32)
    return (latents, cache[None])


def solution(mesh):
    return jax.shard_map(
        body,
        mesh=mesh,
        in_specs=(
            P("req", "patch", None),
            P("section", ("patch", "req"), None),
            P("section", ("patch", "req"), None),
            P("section", "req", None, None),
            P("section", "req", None, None),
            P("req"),
            P("section", "req", "patch", None),
            P("section", "req", "patch", None),
            P("section", "req", "patch"),
            P("req", None),
        ),
        out_specs=(P("req", "patch", "section"), P("section", "req", "patch", None)),
        check_vma=False,
    )
```

```python
import jax
import jax.numpy as jnp
from jax import lax
from jax.experimental import pallas as pl
from jax.experimental.pallas import tpu as pltpu
from jax.sharding import PartitionSpec as P

HEADS = 12


norm_eps = 1e-06
score_scale = 0.125


def shifted(block, axis, distance):
    devices = range(lax.axis_size(axis))
    route = [(i - distance, i) for i in devices if i - distance in devices]
    return lax.ppermute(block, axis, route)


def rotated(block, axis, distance):
    size = lax.axis_size(axis)
    return lax.ppermute(block, axis, [(i, (i + distance) % size) for i in range(size)])


def modulate(row_block, shift_row, scale_row):
    values = row_block.astype(jnp.float32)
    centre = values - jnp.mean(values, axis=-1, keepdims=True)
    spread = jnp.mean(centre * centre, axis=-1, keepdims=True)
    return (centre * lax.rsqrt(spread + norm_eps) * (1.0 + scale_row) + shift_row).astype(
        jnp.bfloat16
    )


def attend(queries, key_rows, value_rows, usable):
    row_count = queries.shape[0]
    feature_count = queries.shape[1]
    query_heads = queries.reshape(row_count, HEADS, feature_count // HEADS)
    key_heads = key_rows.reshape(key_rows.shape[0], HEADS, feature_count // HEADS)
    value_heads = value_rows.reshape(value_rows.shape[0], HEADS, feature_count // HEADS)
    scores = (
        jnp.einsum("qhd,khd->hqk", query_heads, key_heads, preferred_element_type=jnp.float32)
        * score_scale
    )
    scores = jnp.where(usable[None, None, :], scores, -1e30)
    row_max = jnp.max(scores, axis=-1, keepdims=True)
    exp_scores = jnp.exp(scores - row_max)
    soft_weights = (exp_scores / jnp.sum(exp_scores, axis=-1, keepdims=True)).astype(jnp.bfloat16)
    attended = jnp.einsum(
        "hqk,khd->qhd", soft_weights, value_heads, preferred_element_type=jnp.float32
    )
    return attended.reshape(row_count, feature_count).astype(jnp.bfloat16)


def attention_kernel(count_ref, q_ref, fk_ref, fv_ref, tk_ref, tv_ref, *refs):
    *other_refs, keep_ref, rk_ref, rv_ref, out_ref = refs
    text_count = count_ref[0]
    lanes = q_ref.shape[1]
    half = lanes // 2
    queries = q_ref[...] * jnp.asarray(score_scale, q_ref.dtype)
    lane = lax.broadcasted_iota(jnp.int32, queries.shape, 1)
    text_slot = lax.broadcasted_iota(jnp.int32, (queries.shape[0], tk_ref.shape[0]), 1)
    kept = keep_ref[...] > 0
    other_rows = other_refs[0].shape[0]
    blocks = [(tk_ref, tv_ref, "text"), (fk_ref, fv_ref, None)]
    for number in range(len(other_refs) // 2):
        blocks.append((other_refs[2 * number], other_refs[2 * number + 1], number))
    blocks.append((rk_ref, rv_ref, None))
    result = jnp.zeros(out_ref.shape, jnp.float32)
    for head in range(2):
        own = (lane >= half) if head else (lane < half)
        masked = jnp.where(own, queries, jnp.zeros_like(queries))
        scores = []
        for key_ref, _, mask in blocks:
            s = lax.dot_general(
                masked, key_ref[...], (((1,), (1,)), ((), ())), preferred_element_type=jnp.float32
            )
            if mask == "text":
                s = jnp.where(text_slot < text_count, s, -1e30)
            elif mask is not None:
                s = jnp.where(kept[:, mask * other_rows : (mask + 1) * other_rows], s, -1e30)
            scores.append(s)
        row_max = scores[0].max(axis=1, keepdims=True)
        for s in scores[1:]:
            row_max = jnp.maximum(row_max, s.max(axis=1, keepdims=True))
        exps = [jnp.exp(s - row_max) for s in scores]
        total = exps[0].sum(axis=1, keepdims=True)
        for e in exps[1:]:
            total = total + e.sum(axis=1, keepdims=True)
        inverse = 1.0 / total
        part = jnp.zeros(out_ref.shape, jnp.float32)
        for e, (_, value_ref, _) in zip(exps, blocks):
            weights = (e * inverse).astype(jnp.bfloat16)
            part = part + jnp.dot(weights, value_ref[...], preferred_element_type=jnp.float32)
        result = jnp.where(own, part, result)
    out_ref[...] = result.astype(out_ref.dtype)


def fused_attention(projected, text_all, arrivals, keep_all, redone_all, text_count, slot, patch_rows):
    rows = projected.shape[0]
    width = text_all.shape[2] // 2
    pairs = width // 128
    text_slots = text_all.shape[1]
    keep_width = keep_all.shape[2]
    redone_count = redone_all.shape[1]

    def col(offset, height):
        return pl.BlockSpec((height, 128), lambda j, c: (0, j + offset))

    def slotted(offset, height):
        return pl.BlockSpec((None, height, 128), lambda j, c: (c[1], 0, j + offset))

    arrival_specs = []
    for _ in arrivals:
        arrival_specs += [slotted(0, patch_rows), slotted(pairs, patch_rows)]
    grid_spec = pltpu.PrefetchScalarGridSpec(
        num_scalar_prefetch=1,
        grid=(pairs,),
        in_specs=[
            col(0, rows),
            col(pairs, rows),
            col(2 * pairs, rows),
            slotted(0, text_slots),
            slotted(pairs, text_slots),
            *arrival_specs,
            pl.BlockSpec((None, 1, keep_width), lambda j, c: (c[1], 0, 0)),
            slotted(0, redone_count),
            slotted(pairs, redone_count),
        ],
        out_specs=col(0, rows),
    )
    keys = text_slots + rows + keep_width + redone_count
    arrival_args = []
    for arrival in arrivals:
        arrival_args += [arrival, arrival]
    scalars = jnp.stack([text_count, slot]).astype(jnp.int32)
    return pl.pallas_call(
        attention_kernel,
        grid_spec=grid_spec,
        out_shape=jax.ShapeDtypeStruct((rows, width), jnp.bfloat16),
        cost_estimate=pl.CostEstimate(
            flops=4 * rows * keys * width * 2,
            transcendentals=rows * keys * HEADS,
            bytes_accessed=2 * (rows * 3 * width + keys * 2 * width),
        ),
    )(
        scalars,
        projected,
        projected,
        projected,
        text_all,
        text_all,
        *arrival_args,
        keep_all,
        redone_all,
        redone_all,
    )


def gather_weights(w_qkv, w_out):
    qkv_shard = w_qkv[0]
    out_shard = w_out[0]
    qkv_rows, qkv_cols = qkv_shard.shape
    out_rows, out_cols = out_shard.shape
    out_folded = out_shard.reshape(-1, qkv_cols)
    chunk = jnp.concatenate([qkv_shard, out_folded], axis=0)
    chunk_rows = chunk.shape[0]
    gathered = lax.all_gather(chunk, "patch", axis=0, tiled=True)
    gathered = lax.all_gather(gathered, "req", axis=0, tiled=True)
    patches = lax.axis_size("patch")
    requests = lax.axis_size("req")
    blocks = gathered.reshape(requests, patches, chunk_rows, qkv_cols)
    full_out = (
        blocks[:, :, qkv_rows:].transpose(1, 0, 2, 3).reshape(patches * requests, -1)
    ).reshape(-1, out_cols)
    return gathered, full_out


def spread_columns(values, patches, requests, chunk_rows):
    count = values.shape[0]
    values = values.reshape(count, patches, requests, -1).transpose(0, 2, 1, 3)
    pad = chunk_rows - values.shape[3]
    values = jnp.pad(values, ((0, 0), (0, 0), (0, 0), (0, pad)))
    return values.reshape(count, -1)


def body(
    hidden,
    w_qkv,
    w_out,
    modulation,
    text_kv,
    text_lengths,
    stale_kv,
    held_hidden,
    recompute_rows,
    coefficients,
):
    section_index = lax.axis_index("section")
    patch_count = lax.axis_size("patch")
    request_count = hidden.shape[0]
    patch_rows = hidden.shape[1]
    model_width = hidden.shape[2]
    held_count = held_hidden.shape[2]
    text_slots = text_kv.shape[2]

    index_row = jnp.zeros((request_count, 1, model_width), jnp.bfloat16)
    index_row = index_row.at[:, 0, :held_count].set(recompute_rows[0].astype(jnp.bfloat16))
    payload = jnp.concatenate([stale_kv[0], held_hidden[0], index_row], axis=1)
    arrivals = [rotated(payload, "patch", distance) for distance in range(1, patch_count)]

    full_qkv, full_out = gather_weights(w_qkv, w_out)
    head_width = full_out.shape[0]
    key_weights = full_qkv[:, head_width:]
    patches = lax.axis_size("patch")
    requests = lax.axis_size("req")
    chunk_rows = full_qkv.shape[0] // (patches * requests)

    def spread(values):
        return spread_columns(values, patches, requests, chunk_rows)

    keeps, redones = [], []
    for slot in range(request_count):
        mod_rows = modulation[0, slot]
        held_rows = jnp.concatenate(
            [arrival[slot, patch_rows : patch_rows + held_count] for arrival in arrivals], axis=0
        )
        redo_index = jnp.concatenate(
            [
                arrival[slot, patch_rows + held_count, :held_count].astype(jnp.int32)
                + number * patch_rows
                for number, arrival in enumerate(arrivals)
            ]
        )
        replaced = jnp.any(
            redo_index[:, None] == jnp.arange(len(arrivals) * patch_rows)[None, :], axis=0
        )
        held_norm = modulate(held_rows, mod_rows[0], mod_rows[1])
        redone = jnp.dot(spread(held_norm), key_weights, preferred_element_type=jnp.float32).astype(
            jnp.bfloat16
        )
        keeps.append(jnp.where(replaced, 0, 1).astype(jnp.int32)[None, :])
        redones.append(redone)
    keeps = jnp.stack(keeps)
    redones = jnp.stack(redones)

    def process(layer_input, slot_index):
        mod_rows = lax.dynamic_index_in_dim(modulation[0], slot_index, 0, keepdims=False)
        text_count = lax.dynamic_index_in_dim(text_lengths, slot_index, 0, keepdims=False)
        normed = modulate(layer_input, mod_rows[0], mod_rows[1])
        projected = jnp.dot(spread(normed), full_qkv, preferred_element_type=jnp.float32).astype(
            jnp.bfloat16
        )
        fresh_rows = projected[:, head_width:]
        attended = fused_attention(
            projected, text_kv[0], arrivals, keeps, redones, text_count, slot_index, patch_rows
        )
        update = jnp.dot(attended, full_out, preferred_element_type=jnp.float32)
        layer_out = (layer_input.astype(jnp.float32) + mod_rows[2] * update).astype(jnp.bfloat16)
        return layer_out, fresh_rows

    first_section = section_index == 0
    half_width = model_width // 2

    out_1, fresh_1 = process(hidden[0], jnp.int32(0))
    received_1 = shifted(out_1, "section", 1)
    input_2 = jnp.where(first_section, hidden[1], received_1)
    out_2, fresh_2 = process(input_2, jnp.where(first_section, 1, 0).astype(jnp.int32))
    returned_a = shifted(out_2[:, :half_width], "section", -1)
    received_2 = shifted(out_2, "section", 1)
    out_3, fresh_3 = process(received_2, jnp.int32(1))
    returned_b = shifted(out_3[:, :half_width], "section", -1)

    cache = jnp.stack(
        [jnp.where(first_section, fresh_1, fresh_2), jnp.where(first_section, fresh_2, fresh_3)]
    )
    last_out = jnp.stack([out_2, out_3])
    returned = jnp.stack([returned_a, returned_b])
    own_half = jnp.where(first_section, returned, last_out[:, :, half_width:])
    source_half = lax.dynamic_slice_in_dim(hidden, section_index * half_width, half_width, 2)
    latents = coefficients[:, 0][:, None, None] * source_half.astype(jnp.float32) + coefficients[
        :, 1
    ][:, None, None] * own_half.astype(jnp.float32)
    return (latents, cache[None])


def solution(mesh):
    return jax.shard_map(
        body,
        mesh=mesh,
        in_specs=(
            P("req", "patch", None),
            P("section", ("patch", "req"), None),
            P("section", ("patch", "req"), None),
            P("section", "req", None, None),
            P("section", "req", None, None),
            P("req"),
            P("section", "req", "patch", None),
            P("section", "req", "patch", None),
            P("section", "req", "patch"),
            P("req", None),
        ),
        out_specs=(P("req", "patch", "section"), P("section", "req", "patch", None)),
        check_vma=False,
    )
```

```python
import jax
import jax.numpy as jnp
from jax import lax
from jax.experimental import pallas as pl
from jax.experimental.pallas import tpu as pltpu
from jax.sharding import PartitionSpec as P

HEADS = 12


norm_eps = 1e-06
score_scale = 0.125


def shifted(block, axis, distance):
    devices = range(lax.axis_size(axis))
    route = [(i - distance, i) for i in devices if i - distance in devices]
    return lax.ppermute(block, axis, route)


def rotated(block, axis, distance):
    size = lax.axis_size(axis)
    return lax.ppermute(block, axis, [(i, (i + distance) % size) for i in range(size)])


def modulate(row_block, shift_row, scale_row):
    values = row_block.astype(jnp.float32)
    centre = values - jnp.mean(values, axis=-1, keepdims=True)
    spread = jnp.mean(centre * centre, axis=-1, keepdims=True)
    return (centre * lax.rsqrt(spread + norm_eps) * (1.0 + scale_row) + shift_row).astype(
        jnp.bfloat16
    )


def attend(queries, key_rows, value_rows, usable):
    row_count = queries.shape[0]
    feature_count = queries.shape[1]
    query_heads = queries.reshape(row_count, HEADS, feature_count // HEADS)
    key_heads = key_rows.reshape(key_rows.shape[0], HEADS, feature_count // HEADS)
    value_heads = value_rows.reshape(value_rows.shape[0], HEADS, feature_count // HEADS)
    scores = (
        jnp.einsum("qhd,khd->hqk", query_heads, key_heads, preferred_element_type=jnp.float32)
        * score_scale
    )
    scores = jnp.where(usable[None, None, :], scores, -1e30)
    row_max = jnp.max(scores, axis=-1, keepdims=True)
    exp_scores = jnp.exp(scores - row_max)
    soft_weights = (exp_scores / jnp.sum(exp_scores, axis=-1, keepdims=True)).astype(jnp.bfloat16)
    attended = jnp.einsum(
        "hqk,khd->qhd", soft_weights, value_heads, preferred_element_type=jnp.float32
    )
    return attended.reshape(row_count, feature_count).astype(jnp.bfloat16)


def attention_kernel(count_ref, q_ref, fk_ref, fv_ref, tk_ref, tv_ref, *refs):
    *other_refs, keep_ref, rk_ref, rv_ref, out_ref = refs
    text_count = count_ref[0]
    lanes = q_ref.shape[1]
    half = lanes // 2
    queries = q_ref[...] * jnp.asarray(score_scale, q_ref.dtype)
    lane = lax.broadcasted_iota(jnp.int32, queries.shape, 1)
    text_slot = lax.broadcasted_iota(jnp.int32, (queries.shape[0], tk_ref.shape[0]), 1)
    kept = keep_ref[...] > 0
    other_rows = other_refs[0].shape[0]
    blocks = [(tk_ref, tv_ref, "text"), (fk_ref, fv_ref, None)]
    for number in range(len(other_refs) // 2):
        blocks.append((other_refs[2 * number], other_refs[2 * number + 1], number))
    blocks.append((rk_ref, rv_ref, None))
    result = jnp.zeros(out_ref.shape, jnp.float32)
    for head in range(2):
        own = (lane >= half) if head else (lane < half)
        masked = jnp.where(own, queries, jnp.zeros_like(queries))
        scores = []
        for key_ref, _, mask in blocks:
            s = lax.dot_general(
                masked, key_ref[...], (((1,), (1,)), ((), ())), preferred_element_type=jnp.float32
            )
            if mask == "text":
                s = jnp.where(text_slot < text_count, s, -1e30)
            elif mask is not None:
                s = jnp.where(kept[:, mask * other_rows : (mask + 1) * other_rows], s, -1e30)
            scores.append(s)
        row_max = scores[0].max(axis=1, keepdims=True)
        for s in scores[1:]:
            row_max = jnp.maximum(row_max, s.max(axis=1, keepdims=True))
        exps = [jnp.exp(s - row_max) for s in scores]
        total = exps[0].sum(axis=1, keepdims=True)
        for e in exps[1:]:
            total = total + e.sum(axis=1, keepdims=True)
        inverse = 1.0 / total
        part = jnp.zeros(out_ref.shape, jnp.float32)
        for e, (_, value_ref, _) in zip(exps, blocks):
            weights = (e * inverse).astype(jnp.bfloat16)
            part = part + jnp.dot(weights, value_ref[...], preferred_element_type=jnp.float32)
        result = jnp.where(own, part, result)
    out_ref[...] = result.astype(out_ref.dtype)


def fused_attention(projected, text_all, arrivals, keep_all, redone_all, text_count, slot, patch_rows):
    rows = projected.shape[0]
    width = text_all.shape[2] // 2
    pairs = width // 128
    text_slots = text_all.shape[1]
    keep_width = keep_all.shape[2]
    redone_count = redone_all.shape[1]

    def col(offset, height):
        return pl.BlockSpec((height, 128), lambda j, c: (0, j + offset))

    def slotted(offset, height):
        return pl.BlockSpec((None, height, 128), lambda j, c: (c[1], 0, j + offset))

    arrival_specs = []
    for _ in arrivals:
        arrival_specs += [slotted(0, patch_rows), slotted(pairs, patch_rows)]
    grid_spec = pltpu.PrefetchScalarGridSpec(
        num_scalar_prefetch=1,
        grid=(pairs,),
        in_specs=[
            col(0, rows),
            col(pairs, rows),
            col(2 * pairs, rows),
            slotted(0, text_slots),
            slotted(pairs, text_slots),
            *arrival_specs,
            pl.BlockSpec((None, 1, keep_width), lambda j, c: (c[1], 0, 0)),
            slotted(0, redone_count),
            slotted(pairs, redone_count),
        ],
        out_specs=col(0, rows),
    )
    keys = text_slots + rows + keep_width + redone_count
    arrival_args = []
    for arrival in arrivals:
        arrival_args += [arrival, arrival]
    scalars = jnp.stack([text_count, slot]).astype(jnp.int32)
    return pl.pallas_call(
        attention_kernel,
        grid_spec=grid_spec,
        out_shape=jax.ShapeDtypeStruct((rows, width), jnp.bfloat16),
        cost_estimate=pl.CostEstimate(
            flops=4 * rows * keys * width * 2,
            transcendentals=rows * keys * HEADS,
            bytes_accessed=2 * (rows * 3 * width + keys * 2 * width),
        ),
    )(
        scalars,
        projected,
        projected,
        projected,
        text_all,
        text_all,
        *arrival_args,
        keep_all,
        redone_all,
        redone_all,
    )


def gather_weights(w_qkv, w_out):
    qkv_shard = w_qkv[0]
    out_shard = w_out[0]
    qkv_rows, qkv_cols = qkv_shard.shape
    out_rows, out_cols = out_shard.shape
    out_folded = out_shard.reshape(-1, qkv_cols)
    chunk = jnp.concatenate([qkv_shard, out_folded], axis=0)
    chunk_rows = chunk.shape[0]
    gathered = lax.all_gather(chunk, "patch", axis=0, tiled=True)
    gathered = lax.all_gather(gathered, "req", axis=0, tiled=True)
    patches = lax.axis_size("patch")
    requests = lax.axis_size("req")
    blocks = gathered.reshape(requests, patches, chunk_rows, qkv_cols)
    full_out = (
        blocks[:, :, qkv_rows:].transpose(1, 0, 2, 3).reshape(patches * requests, -1)
    ).reshape(-1, out_cols)
    return gathered, full_out


def spread_columns(values, patches, requests, chunk_rows):
    count = values.shape[0]
    values = values.reshape(count, patches, requests, -1).transpose(0, 2, 1, 3)
    pad = chunk_rows - values.shape[3]
    values = jnp.pad(values, ((0, 0), (0, 0), (0, 0), (0, pad)))
    return values.reshape(count, -1)


def body(
    hidden,
    w_qkv,
    w_out,
    modulation,
    text_kv,
    text_lengths,
    stale_kv,
    held_hidden,
    recompute_rows,
    coefficients,
):
    section_index = lax.axis_index("section")
    patch_count = lax.axis_size("patch")
    request_count = hidden.shape[0]
    patch_rows = hidden.shape[1]
    model_width = hidden.shape[2]
    held_count = held_hidden.shape[2]
    text_slots = text_kv.shape[2]

    index_row = jnp.zeros((request_count, 1, model_width), jnp.bfloat16)
    index_row = index_row.at[:, 0, :held_count].set(recompute_rows[0].astype(jnp.bfloat16))
    payload = jnp.concatenate([stale_kv[0], held_hidden[0], index_row], axis=1)
    arrivals = [rotated(payload, "patch", distance) for distance in range(1, patch_count)]

    full_qkv, full_out = gather_weights(w_qkv, w_out)
    head_width = full_out.shape[0]
    key_weights = full_qkv[:, head_width:]
    patches = lax.axis_size("patch")
    requests = lax.axis_size("req")
    chunk_rows = full_qkv.shape[0] // (patches * requests)

    def spread(values):
        return spread_columns(values, patches, requests, chunk_rows)

    keeps, redones = [], []
    for slot in range(request_count):
        mod_rows = modulation[0, slot]
        redo_index = jnp.concatenate(
            [
                arrival[slot, patch_rows + held_count, :held_count].astype(jnp.int32)
                + number * patch_rows
                for number, arrival in enumerate(arrivals)
            ]
        )
        replaced = jnp.any(
            redo_index[:, None] == jnp.arange(len(arrivals) * patch_rows)[None, :], axis=0
        )
        redone = jnp.concatenate(
            [
                jnp.dot(
                    spread(
                        modulate(
                            arrival[slot, patch_rows : patch_rows + held_count],
                            mod_rows[0],
                            mod_rows[1],
                        )
                    ),
                    key_weights,
                    preferred_element_type=jnp.float32,
                ).astype(jnp.bfloat16)
                for arrival in arrivals
            ],
            axis=0,
        )
        keeps.append(jnp.where(replaced, 0, 1).astype(jnp.int32)[None, :])
        redones.append(redone)
    keeps = jnp.stack(keeps)
    redones = jnp.stack(redones)

    def process(layer_input, slot_index):
        mod_rows = lax.dynamic_index_in_dim(modulation[0], slot_index, 0, keepdims=False)
        text_count = lax.dynamic_index_in_dim(text_lengths, slot_index, 0, keepdims=False)
        normed = modulate(layer_input, mod_rows[0], mod_rows[1])
        projected = jnp.dot(spread(normed), full_qkv, preferred_element_type=jnp.float32).astype(
            jnp.bfloat16
        )
        fresh_rows = projected[:, head_width:]
        attended = fused_attention(
            projected, text_kv[0], arrivals, keeps, redones, text_count, slot_index, patch_rows
        )
        update = jnp.dot(attended, full_out, preferred_element_type=jnp.float32)
        layer_out = (layer_input.astype(jnp.float32) + mod_rows[2] * update).astype(jnp.bfloat16)
        return layer_out, fresh_rows

    first_section = section_index == 0
    half_width = model_width // 2

    out_1, fresh_1 = process(hidden[0], jnp.int32(0))
    received_1 = shifted(out_1, "section", 1)
    input_2 = jnp.where(first_section, hidden[1], received_1)
    out_2, fresh_2 = process(input_2, jnp.where(first_section, 1, 0).astype(jnp.int32))
    returned_a = shifted(out_2[:, :half_width], "section", -1)
    received_2 = shifted(out_2, "section", 1)
    out_3, fresh_3 = process(received_2, jnp.int32(1))
    returned_b = shifted(out_3[:, :half_width], "section", -1)

    cache = jnp.stack(
        [jnp.where(first_section, fresh_1, fresh_2), jnp.where(first_section, fresh_2, fresh_3)]
    )
    last_out = jnp.stack([out_2, out_3])
    returned = jnp.stack([returned_a, returned_b])
    own_half = jnp.where(first_section, returned, last_out[:, :, half_width:])
    source_half = lax.dynamic_slice_in_dim(hidden, section_index * half_width, half_width, 2)
    latents = coefficients[:, 0][:, None, None] * source_half.astype(jnp.float32) + coefficients[
        :, 1
    ][:, None, None] * own_half.astype(jnp.float32)
    return (latents, cache[None])


def solution(mesh):
    return jax.shard_map(
        body,
        mesh=mesh,
        in_specs=(
            P("req", "patch", None),
            P("section", ("patch", "req"), None),
            P("section", ("patch", "req"), None),
            P("section", "req", None, None),
            P("section", "req", None, None),
            P("req"),
            P("section", "req", "patch", None),
            P("section", "req", "patch", None),
            P("section", "req", "patch"),
            P("req", None),
        ),
        out_specs=(P("req", "patch", "section"), P("section", "req", "patch", None)),
        check_vma=False,
    )
```
